256 devices in a mesh: dp: 4 (over y_lo, core), seq: 64 (over x, y_hi, z).
Axes of the slice: x: 4, y: 4 (y_hi: 2, y_lo: 2; y = y_hi * 2 + y_lo), z: 8, core: 2. Of those that a mesh axis runs over, the one named last changes fastest.
Arguments:
- inputs: bfloat16 [8, 65536, 768], P('dp', 'seq'), may hold values from -6 to 6
- cotangent: bfloat16 [8, 65536, 768], P('dp', 'seq'), may hold values from -6 to 6
- control: int32 [8], P('dp'), may hold values from 0 to 15
- table_in: float32 [16, 768], replicated, may hold values from 0.3 to 3
- table_out: float32 [16, 768], replicated, may hold values from 0.3 to 3
- factor_one: bfloat16 [256, 256, 256], P('seq'), may hold values from -0.375 to 0.375
- second_block_factor: bfloat16 [256, 256, 256], P('seq'), may hold values from -0.375 to 0.375
Outputs:
- grad_inputs: bfloat16 [8, 65536, 768], P('dp', 'seq')
- grad_one: float32 [256, 256, 256], P('seq')
- second_factor_gradient: float32 [256, 256, 256], P('seq')
The draws below stay inside these ranges and needn't reach their ends.
All inputs are finite; a program needn't handle non-finite values.
Results may differ from the reference program's by a relative error of at most 0.0072.
Values may be sent and summed in bfloat16 or wider, within the bound.
No kernel may reach another device: no remote copies, remote signals or barrier semaphores. Data moves between devices by JAX's collectives and lax.ppermute only.
A program may use at most 64 MiB of HBM per device.

```python
import math
import jax
import jax.numpy as jnp
from jax import lax

D = 768
NB = 256
NTAB = 16
IMAGES = 8
L = 65536


def plant(values, rng, smallest, top_value):
    longest = values.shape.index(max(values.shape))
    spots = []
    for shift in (0, 1):
        where = [jax.random.randint(jax.random.fold_in(rng, axis), (), 0, length) for axis, length in enumerate(values.shape)]
        where[longest] = (where[longest] + shift) % values.shape[longest]
        spots.append(tuple(where))
    return values.at[spots[0]].set(smallest).at[spots[1]].set(top_value)


def levels(stream_key, shape, pieces, smallest, largest):
    factor_of, own = 1.0, jax.random.fold_in(stream_key, 6)
    for axis_at, parts in pieces:
        heights = jnp.exp(jax.random.uniform(jax.random.fold_in(own, axis_at), (parts,), jnp.float32, smallest / len(pieces), largest / len(pieces)))
        factor_of = factor_of * jnp.repeat(heights, shape[axis_at] // parts).reshape([-1 if axis == axis_at else 1 for axis in range(len(shape))])
    return factor_of


def scatter_about(own_key, shape, width, bound, pieces=(), held_as=jnp.bfloat16):
    values = width * jax.random.normal(own_key, shape, jnp.float32)
    if pieces:
        values = values * levels(own_key, shape, pieces, -0.22, 0.18)
    return jnp.clip(values, -bound, bound).astype(held_as)


def setup_inputs(seed: int = 0) -> dict:
    key_of = jax.random.split(jax.random.key(seed), 8)
    inputs = scatter_about(key_of[0], (IMAGES, L, D), 1.0, 6.0, ((0, 4), (1, 64)))
    cotangent = scatter_about(key_of[1], (IMAGES, L, D), 1.0, 6.0, ((0, 4), (1, 64)))
    control = plant(jax.random.randint(key_of[2], (IMAGES,), 0, NTAB), jax.random.fold_in(key_of[2], 1), 0, NTAB - 1).astype(jnp.int32)
    table_in = jnp.clip(jnp.exp(jax.random.uniform(key_of[3], (NTAB, D), jnp.float32, math.log(0.3), math.log(3.0))), 0.3, 3.0)
    table_out = jnp.clip(jnp.exp(jax.random.uniform(key_of[4], (NTAB, D), jnp.float32, math.log(0.3), math.log(3.0))), 0.3, 3.0)
    factor_one = scatter_about(key_of[5], (NB, NB, NB), NB ** -0.5, 0.375, ((0, 64),))
    second_block_factor = scatter_about(key_of[6], (NB, NB, NB), NB ** -0.5, 0.375, ((0, 64),))
    return dict(inputs=inputs, cotangent=cotangent, control=control, table_in=table_in, table_out=table_out, factor_one=factor_one, second_block_factor=second_block_factor)


def reference(inputs, cotangent, control, table_in, table_out, factor_one, second_block_factor):
    first = factor_one.astype(jnp.float32)
    second_product = second_block_factor.astype(jnp.float32)

    def one_image(carry, item):
        acc_one, second_accumulator = carry
        source, upstream, index = item
        gate_in = table_in[index]
        gate_out = table_out[index]
        scaled = (source.reshape(NB, NB, D).astype(jnp.float32) * gate_in).astype(jnp.bfloat16)
        first_mixed_output = jnp.einsum('acb,abd->acd', first, scaled.astype(jnp.float32)).astype(jnp.bfloat16)
        second_mixed_output = jnp.einsum('goi,igy->goy', second_product, first_mixed_output.astype(jnp.float32))
        logistic = jax.nn.sigmoid(second_mixed_output)
        upstream_grid = upstream.reshape(NB, NB, D).astype(jnp.float32)
        value_gradient = (upstream_grid * gate_out * logistic * (1.0 + second_mixed_output * (1.0 - logistic))).astype(jnp.bfloat16)
        second_accumulator = second_accumulator + jnp.einsum('jnu,mju->jnm', value_gradient.astype(jnp.float32), first_mixed_output.astype(jnp.float32))
        mixed_gradient = jnp.einsum('zyf,zyl->fzl', second_product, value_gradient.astype(jnp.float32)).astype(jnp.bfloat16)
        acc_one = acc_one + jnp.einsum('acd,abd->acb', mixed_gradient.astype(jnp.float32), scaled.astype(jnp.float32))
        back_sum = jnp.einsum('acb,acd->abd', first, mixed_gradient.astype(jnp.float32))
        grad_x = (back_sum * gate_in).astype(jnp.bfloat16).reshape(NB * NB, D)
        return (acc_one, second_accumulator), grad_x

    zeros = jnp.zeros((NB, NB, NB), jnp.float32)
    (grad_one, second_factor_gradient), grad_inputs = lax.scan(one_image, (zeros, zeros), (inputs, cotangent, control))
    return grad_inputs, grad_one, second_factor_gradient
```

```python
import jax
import jax.numpy as jnp
from jax import lax
from jax.sharding import PartitionSpec as P


def dp_sum(x, n_dp):
    step = 1
    while step < n_dp:
        perm = [(i, i ^ step) for i in range(n_dp)]
        x = x + lax.ppermute(x, "dp", perm)
        step *= 2
    return x


def on_device(inputs, cotangent, control, table_in, table_out, factor_one, second_block_factor, n_dp):
    f32, bf16 = jnp.float32, jnp.bfloat16
    images, rows, width = inputs.shape
    own, blocks, _ = factor_one.shape
    n_seq = blocks // own
    gate_in = jnp.take(table_in, control, axis=0)
    gate_out = jnp.take(table_out, control, axis=0)
    scaled = (
        inputs.reshape(images, own, blocks, width).astype(f32) * gate_in[:, None, None, :]
    ).astype(bf16)
    f1 = factor_one.reshape(own, n_seq, own, blocks)
    upstream = cotangent.reshape(images, own, blocks, width)

    recv1 = []
    for j in range(own):
        mixed = jnp.einsum(
            "asb,iabd->said", f1[:, :, j, :], scaled, preferred_element_type=f32
        ).astype(bf16)
        recv1.append(lax.all_to_all(mixed, "seq", 0, 0, tiled=True))

    recv2 = []
    sfg = []
    for j in range(own):
        got = recv1[j].reshape(blocks, images, width)
        f2 = second_block_factor[j]
        mixed_b = jnp.einsum("pa,aid->ipd", f2, got, preferred_element_type=f32)
        logistic = jax.nn.sigmoid(mixed_b)
        value_gradient = (
            upstream[:, j]
            * gate_out[:, None, :]
            * logistic
            * (1.0 + mixed_b * (1.0 - logistic))
        ).astype(bf16)
        sfg.append(
            dp_sum(jnp.einsum("ipd,aid->pa", value_gradient, got, preferred_element_type=f32), n_dp)
        )
        grad_a = jnp.einsum("pa,ipd->aid", f2, value_gradient, preferred_element_type=f32).astype(bf16)
        recv2.append(
            lax.all_to_all(grad_a.reshape(n_seq, own, images, width), "seq", 0, 0, tiled=True)
        )

    grad_one = []
    for j in range(own):
        part = jnp.einsum("said,iabd->asb", recv2[j], scaled, preferred_element_type=f32)
        grad_one.append(dp_sum(part, n_dp))
    grad_one = jnp.stack(grad_one, axis=2).reshape(own, blocks, blocks)
    grads = jnp.stack(recv2, axis=2)
    back_sum = jnp.einsum("asjb,sajid->iabd", f1, grads, preferred_element_type=f32)
    grad_inputs = (
        (back_sum * gate_in[:, None, None, :]).astype(bf16).reshape(images, rows, width)
    )
    second_factor_gradient = jnp.stack(sfg, axis=0)
    return (grad_inputs, grad_one, second_factor_gradient)


def solution(mesh):
    n_dp = mesh.shape["dp"]

    def fn(*args):
        return on_device(*args, n_dp=n_dp)

    return jax.shard_map(
        fn,
        mesh=mesh,
        in_specs=(
            P("dp", "seq", None),
            P("dp", "seq", None),
            P("dp"),
            P(),
            P(),
            P("seq", None, None),
            P("seq", None, None),
        ),
        out_specs=(P("dp", "seq", None), P("seq", None, None), P("seq", None, None)),
        check_vma=False,
    )
```

```python
import jax
import jax.numpy as jnp
from jax import lax
from jax.sharding import PartitionSpec as P

CHUNKS = 2


def dp_sum(x, n_dp):
    step = 1
    while step < n_dp:
        perm = [(i, i ^ step) for i in range(n_dp)]
        x = x + lax.ppermute(x, "dp", perm)
        step *= 2
    return x


def on_device(inputs, cotangent, control, table_in, table_out, factor_one, second_block_factor, n_dp):
    f32, bf16 = jnp.float32, jnp.bfloat16
    images, rows, width = inputs.shape
    own, blocks, _ = factor_one.shape
    n_seq = blocks // own
    per = own // CHUNKS
    gate_in = jnp.take(table_in, control, axis=0)
    gate_out = jnp.take(table_out, control, axis=0)
    scaled = (
        inputs.reshape(images, own, blocks, width).astype(f32) * gate_in[:, None, None, :]
    ).astype(bf16)
    f1 = factor_one.reshape(own, n_seq, own, blocks)
    upstream = cotangent.reshape(images, own, blocks, width)

    recv1 = []
    for k in range(CHUNKS):
        mixed = jnp.einsum(
            "asjb,iabd->sajid", f1[:, :, k * per:(k + 1) * per, :], scaled, preferred_element_type=f32
        ).astype(bf16)
        recv1.append(lax.all_to_all(mixed, "seq", 0, 0, tiled=True))

    recv2 = []
    sfg = []
    for k in range(CHUNKS):
        sends = []
        for jj in range(per):
            j = k * per + jj
            got = recv1[k][:, :, jj].reshape(blocks, images, width)
            f2 = second_block_factor[j]
            mixed_b = jnp.einsum("pa,aid->pid", f2, got, preferred_element_type=f32)
            logistic = jax.nn.sigmoid(mixed_b)
            up = jnp.transpose(upstream[:, j], (1, 0, 2))
            value_gradient = (
                up * gate_out[None, :, :] * logistic * (1.0 + mixed_b * (1.0 - logistic))
            ).astype(bf16)
            sfg.append(
                dp_sum(
                    jnp.einsum("pid,aid->pa", value_gradient, got, preferred_element_type=f32), n_dp
                )
            )
            sends.append(
                jnp.einsum("pa,pid->aid", f2, value_gradient, preferred_element_type=f32).astype(bf16)
            )
        send = jnp.stack(sends, axis=1).reshape(n_seq, own, per, images, width)
        recv2.append(lax.all_to_all(send, "seq", 0, 0, tiled=True))

    grad_one = []
    back_sum = None
    for k in range(CHUNKS):
        part = jnp.einsum("sajid,iabd->asjb", recv2[k], scaled, preferred_element_type=f32)
        grad_one.append(dp_sum(part, n_dp))
        term = jnp.einsum(
            "asjb,sajid->iabd", f1[:, :, k * per:(k + 1) * per, :], recv2[k], preferred_element_type=f32
        )
        back_sum = term if back_sum is None else back_sum + term
    grad_one = jnp.concatenate(grad_one, axis=2).reshape(own, blocks, blocks)
    grad_inputs = (
        (back_sum * gate_in[:, None, None, :]).astype(bf16).reshape(images, rows, width)
    )
    second_factor_gradient = jnp.stack(sfg, axis=0)
    return (grad_inputs, grad_one, second_factor_gradient)


def solution(mesh):
    n_dp = mesh.shape["dp"]

    def fn(*args):
        return on_device(*args, n_dp=n_dp)

    return jax.shard_map(
        fn,
        mesh=mesh,
        in_specs=(
            P("dp", "seq", None),
            P("dp", "seq", None),
            P("dp"),
            P(),
            P(),
            P("seq", None, None),
            P("seq", None, None),
        ),
        out_specs=(P("dp", "seq", None), P("seq", None, None), P("seq", None, None)),
        check_vma=False,
    )
```

```python
import jax
import jax.numpy as jnp
from jax import lax
from jax.sharding import PartitionSpec as P

CHUNKS = 2


def dp_sum(x, n_dp):
    step = 1
    while step < n_dp:
        perm = [(i, i ^ step) for i in range(n_dp)]
        x = x + lax.ppermute(x, "dp", perm)
        step *= 2
    return x


def dp_sum_halves(x, n_dp):
    if n_dp != 4 or x.shape[0] % 2:
        return dp_sum(x, n_dp)
    core = lax.axis_index("dp") % 2
    x = x + lax.ppermute(x, "dp", [(i, i ^ 1) for i in range(n_dp)])
    halves = x.reshape((2, x.shape[0] // 2) + x.shape[1:])
    mine = lax.dynamic_index_in_dim(halves, core, 0, keepdims=False)
    mine = mine + lax.ppermute(mine, "dp", [(i, i ^ 2) for i in range(n_dp)])
    other = lax.ppermute(mine, "dp", [(i, i ^ 1) for i in range(n_dp)])
    first = jnp.where(core == 0, mine, other)
    second = jnp.where(core == 0, other, mine)
    return jnp.concatenate([first, second], axis=0)


def on_device(inputs, cotangent, control, table_in, table_out, factor_one, second_block_factor, n_dp):
    f32, bf16 = jnp.float32, jnp.bfloat16
    images, rows, width = inputs.shape
    own, blocks, _ = factor_one.shape
    n_seq = blocks // own
    per = own // CHUNKS
    tables = table_in.shape[0]
    one_hot = (control[:, None] == jnp.arange(tables, dtype=jnp.int32)[None, :]).astype(f32)
    gate_in = jnp.dot(one_hot, table_in, precision=lax.Precision.HIGHEST)
    gate_out = jnp.dot(one_hot, table_out, precision=lax.Precision.HIGHEST)
    scaled = (
        inputs.reshape(images, own, blocks, width).astype(f32) * gate_in[:, None, None, :]
    ).astype(bf16)
    f1 = factor_one.reshape(own, n_seq, own, blocks)
    upstream = cotangent.reshape(images, own, blocks, width)

    recv1 = []
    for k in range(CHUNKS):
        mixed = jnp.einsum(
            "asjb,iabd->sajid", f1[:, :, k * per:(k + 1) * per, :], scaled, preferred_element_type=f32
        ).astype(bf16)
        recv1.append(lax.all_to_all(mixed, "seq", 0, 0, tiled=True))

    recv2 = []
    sfg = []
    for k in range(CHUNKS):
        sends = []
        for jj in range(per):
            j = k * per + jj
            got = recv1[k][:, :, jj].reshape(blocks, images, width)
            f2 = second_block_factor[j]
            mixed_b = jnp.einsum("pa,aid->pid", f2, got, preferred_element_type=f32)
            logistic = jax.nn.sigmoid(mixed_b)
            up = jnp.transpose(upstream[:, j], (1, 0, 2))
            value_gradient = (
                up * gate_out[None, :, :] * logistic * (1.0 + mixed_b * (1.0 - logistic))
            ).astype(bf16)
            sfg.append(jnp.einsum("pid,aid->pa", value_gradient, got, preferred_element_type=f32))
            sends.append(
                jnp.einsum("pa,pid->aid", f2, value_gradient, preferred_element_type=f32).astype(bf16)
            )
        send = jnp.stack(sends, axis=1).reshape(n_seq, own, per, images, width)
        if k == CHUNKS - 1:
            sfg, send = lax.optimization_barrier((jnp.stack(sfg, axis=0), send))
        recv2.append(lax.all_to_all(send, "seq", 0, 0, tiled=True))

    grad_one = []
    back_sum = None
    for k in range(CHUNKS):
        part = jnp.einsum("sajid,iabd->asjb", recv2[k], scaled, preferred_element_type=f32)
        grad_one.append(dp_sum_halves(part, n_dp))
        term = jnp.einsum(
            "asjb,sajid->iabd", f1[:, :, k * per:(k + 1) * per, :], recv2[k], preferred_element_type=f32
        )
        back_sum = term if back_sum is None else back_sum + term
    grad_one = jnp.concatenate(grad_one, axis=2).reshape(own, blocks, blocks)
    grad_inputs = (
        (back_sum * gate_in[:, None, None, :]).astype(bf16).reshape(images, rows, width)
    )
    second_factor_gradient = dp_sum_halves(sfg, n_dp)
    return (grad_inputs, grad_one, second_factor_gradient)


def solution(mesh):
    n_dp = mesh.shape["dp"]

    def fn(*args):
        return on_device(*args, n_dp=n_dp)

    return jax.shard_map(
        fn,
        mesh=mesh,
        in_specs=(
            P("dp", "seq", None),
            P("dp", "seq", None),
            P("dp"),
            P(),
            P(),
            P("seq", None, None),
            P("seq", None, None),
        ),
        out_specs=(P("dp", "seq", None), P("seq", None, None), P("seq", None, None)),
        check_vma=False,
    )
```

```python
import jax
import jax.numpy as jnp
from jax import lax
from jax.sharding import PartitionSpec as P

CHUNKS = 2


def dp_sum(x, n_dp):
    step = 1
    while step < n_dp:
        perm = [(i, i ^ step) for i in range(n_dp)]
        x = x + lax.ppermute(x, "dp", perm)
        step *= 2
    return x


def dp_sum_halves(x, n_dp):
    if n_dp != 4 or x.shape[0] % 2:
        return dp_sum(x, n_dp)
    core = lax.axis_index("dp") % 2
    x = x + lax.ppermute(x, "dp", [(i, i ^ 1) for i in range(n_dp)])
    halves = x.reshape((2, x.shape[0] // 2) + x.shape[1:])
    mine = lax.dynamic_index_in_dim(halves, core, 0, keepdims=False)
    mine = mine + lax.ppermute(mine, "dp", [(i, i ^ 2) for i in range(n_dp)])
    other = lax.ppermute(mine, "dp", [(i, i ^ 1) for i in range(n_dp)])
    first = jnp.where(core == 0, mine, other)
    second = jnp.where(core == 0, other, mine)
    return jnp.concatenate([first, second], axis=0)


def on_device(inputs, cotangent, control, table_in, table_out, factor_one, second_block_factor, n_dp):
    f32, bf16 = jnp.float32, jnp.bfloat16
    images, rows, width = inputs.shape
    own, blocks, _ = factor_one.shape
    n_seq = blocks // own
    per = own // CHUNKS
    tables = table_in.shape[0]
    one_hot = (control[:, None] == jnp.arange(tables, dtype=jnp.int32)[None, :]).astype(f32)
    gate_in = jnp.dot(one_hot, table_in, precision=lax.Precision.HIGHEST)
    gate_out = jnp.dot(one_hot, table_out, precision=lax.Precision.HIGHEST)
    scaled = (
        inputs.reshape(images, own, blocks, width).astype(f32) * gate_in[:, None, None, :]
    ).astype(bf16)
    f1 = factor_one.reshape(own, n_seq, own, blocks)
    upstream = cotangent.reshape(images, own, blocks, width)

    recv1 = []
    for k in range(CHUNKS):
        mixed = jnp.einsum(
            "asjb,iabd->sajid", f1[:, :, k * per:(k + 1) * per, :], scaled, preferred_element_type=f32
        ).astype(bf16)
        recv1.append(lax.all_to_all(mixed, "seq", 0, 0, tiled=True))

    recv2 = []
    sfg = []
    for k in range(CHUNKS):
        got = recv1[k].reshape(blocks, per, images, width)
        f2 = second_block_factor[k * per:(k + 1) * per]
        mixed_b = jnp.einsum("jpa,ajid->jpid", f2, got, preferred_element_type=f32)
        logistic = jax.nn.sigmoid(mixed_b)
        up = jnp.transpose(upstream[:, k * per:(k + 1) * per], (1, 2, 0, 3))
        value_gradient = (
            up * gate_out[None, None, :, :] * logistic * (1.0 + mixed_b * (1.0 - logistic))
        ).astype(bf16)
        part = jnp.einsum("jpid,ajid->jpa", value_gradient, got, preferred_element_type=f32)
        send = jnp.einsum("jpa,jpid->ajid", f2, value_gradient, preferred_element_type=f32).astype(bf16)
        send = send.reshape(n_seq, own, per, images, width)
        part, send = lax.optimization_barrier((part, send))
        sfg.append(dp_sum_halves(part, n_dp))
        recv2.append(lax.all_to_all(send, "seq", 0, 0, tiled=True))

    grad_one = []
    back_sum = None
    for k in range(CHUNKS):
        part = jnp.einsum("sajid,iabd->asjb", recv2[k], scaled, preferred_element_type=f32)
        grad_one.append(dp_sum_halves(part, n_dp))
        term = jnp.einsum(
            "asjb,sajid->iabd", f1[:, :, k * per:(k + 1) * per, :], recv2[k], preferred_element_type=f32
        )
        back_sum = term if back_sum is None else back_sum + term
    grad_one = jnp.concatenate(grad_one, axis=2).reshape(own, blocks, blocks)
    grad_inputs = (
        (back_sum * gate_in[:, None, None, :]).astype(bf16).reshape(images, rows, width)
    )
    second_factor_gradient = jnp.concatenate(sfg, axis=0)
    return (grad_inputs, grad_one, second_factor_gradient)


def solution(mesh):
    n_dp = mesh.shape["dp"]

    def fn(*args):
        return on_device(*args, n_dp=n_dp)

    return jax.shard_map(
        fn,
        mesh=mesh,
        in_specs=(
            P("dp", "seq", None),
            P("dp", "seq", None),
            P("dp"),
            P(),
            P(),
            P("seq", None, None),
            P("seq", None, None),
        ),
        out_specs=(P("dp", "seq", None), P("seq", None, None), P("seq", None, None)),
        check_vma=False,
    )
```

```python
import jax
import jax.numpy as jnp
from jax import lax
from jax.sharding import PartitionSpec as P

CHUNKS = 2


def dp_sum(x, n_dp):
    step = 1
    while step < n_dp:
        perm = [(i, i ^ step) for i in range(n_dp)]
        x = x + lax.ppermute(x, "dp", perm)
        step *= 2
    return x


def dp_sum_halves(x, n_dp, hold=None):
    if n_dp != 4 or x.shape[0] % 2:
        return dp_sum(x, n_dp), hold
    core = lax.axis_index("dp") % 2
    x = x + lax.ppermute(x, "dp", [(i, i ^ 1) for i in range(n_dp)])
    halves = x.reshape((2, x.shape[0] // 2) + x.shape[1:])
    mine = lax.dynamic_index_in_dim(halves, core, 0, keepdims=False)
    if hold is not None:
        mine, hold = lax.optimization_barrier((mine, hold))
    mine = mine + lax.ppermute(mine, "dp", [(i, i ^ 2) for i in range(n_dp)])
    other = lax.ppermute(mine, "dp", [(i, i ^ 1) for i in range(n_dp)])
    first = jnp.where(core == 0, mine, other)
    second = jnp.where(core == 0, other, mine)
    return jnp.concatenate([first, second], axis=0), hold


def on_device(inputs, cotangent, control, table_in, table_out, factor_one, second_block_factor, n_dp):
    f32, bf16 = jnp.float32, jnp.bfloat16
    images, rows, width = inputs.shape
    own, blocks, _ = factor_one.shape
    n_seq = blocks // own
    per = own // CHUNKS
    tables = table_in.shape[0]
    one_hot = (control[:, None] == jnp.arange(tables, dtype=jnp.int32)[None, :]).astype(f32)
    gate_in = jnp.dot(one_hot, table_in, precision=lax.Precision.HIGHEST)
    gate_out = jnp.dot(one_hot, table_out, precision=lax.Precision.HIGHEST)
    scaled = (
        inputs.reshape(images, own, blocks, width).astype(f32) * gate_in[:, None, None, :]
    ).astype(bf16)
    f1 = factor_one.reshape(own, n_seq, own, blocks)
    upstream = cotangent.reshape(images, own, blocks, width)

    recv1 = []
    for k in range(CHUNKS):
        mixed = jnp.einsum(
            "asjb,iabd->sajid", f1[:, :, k * per:(k + 1) * per, :], scaled, preferred_element_type=f32
        ).astype(bf16)
        recv1.append(lax.all_to_all(mixed, "seq", 0, 0, tiled=True))

    recv2 = []
    sfg = []
    for k in range(CHUNKS):
        got = recv1[k].reshape(blocks, per, images, width)
        f2 = second_block_factor[k * per:(k + 1) * per]
        mixed_b = jnp.einsum("jpa,ajid->jpid", f2, got, preferred_element_type=f32)
        logistic = jax.nn.sigmoid(mixed_b)
        up = jnp.transpose(upstream[:, k * per:(k + 1) * per], (1, 2, 0, 3))
        value_gradient = (
            up * gate_out[None, None, :, :] * logistic * (1.0 + mixed_b * (1.0 - logistic))
        ).astype(bf16)
        part = jnp.einsum("jpid,ajid->jpa", value_gradient, got, preferred_element_type=f32)
        send = jnp.einsum("jpa,jpid->ajid", f2, value_gradient, preferred_element_type=f32).astype(bf16)
        send = send.reshape(n_seq, own, per, images, width)
        part, send = lax.optimization_barrier((part, send))
        sfg.append(dp_sum_halves(part, n_dp)[0])
        recv2.append(lax.all_to_all(send, "seq", 0, 0, tiled=True))

    grad_one = []
    back_sum = None
    for k in range(CHUNKS):
        got = recv2[k]
        part = jnp.einsum("sajid,iabd->asjb", got, scaled, preferred_element_type=f32)
        if k == CHUNKS - 1:
            reduced, got = dp_sum_halves(part, n_dp, hold=got)
        else:
            reduced, _ = dp_sum_halves(part, n_dp)
        grad_one.append(reduced)
        term = jnp.einsum(
            "asjb,sajid->iabd", f1[:, :, k * per:(k + 1) * per, :], got, preferred_element_type=f32
        )
        back_sum = term if back_sum is None else back_sum + term
    grad_one = jnp.concatenate(grad_one, axis=2).reshape(own, blocks, blocks)
    grad_inputs = (
        (back_sum * gate_in[:, None, None, :]).astype(bf16).reshape(images, rows, width)
    )
    second_factor_gradient = jnp.concatenate(sfg, axis=0)
    return (grad_inputs, grad_one, second_factor_gradient)


def solution(mesh):
    n_dp = mesh.shape["dp"]

    def fn(*args):
        return on_device(*args, n_dp=n_dp)

    return jax.shard_map(
        fn,
        mesh=mesh,
        in_specs=(
            P("dp", "seq", None),
            P("dp", "seq", None),
            P("dp"),
            P(),
            P(),
            P("seq", None, None),
            P("seq", None, None),
        ),
        out_specs=(P("dp", "seq", None), P("seq", None, None), P("seq", None, None)),
        check_vma=False,
    )
```

```python
import jax
import jax.numpy as jnp
from jax import lax
from jax.sharding import PartitionSpec as P

CHUNKS = 2


def dp_sum(x, n_dp):
    step = 1
    while step < n_dp:
        perm = [(i, i ^ step) for i in range(n_dp)]
        x = x + lax.ppermute(x, "dp", perm)
        step *= 2
    return x


def dp_sum_halves(x, n_dp, hold=None):
    if n_dp != 4 or x.shape[0] % 2:
        return dp_sum(x, n_dp), hold
    core = lax.axis_index("dp") % 2
    x = x + lax.ppermute(x, "dp", [(i, i ^ 1) for i in range(n_dp)])
    halves = x.reshape((2, x.shape[0] // 2) + x.shape[1:])
    mine = lax.dynamic_index_in_dim(halves, core, 0, keepdims=False)
    if hold is not None:
        mine, hold = lax.optimization_barrier((mine, hold))
    mine = mine + lax.ppermute(mine, "dp", [(i, i ^ 2) for i in range(n_dp)])
    other = lax.ppermute(mine, "dp", [(i, i ^ 1) for i in range(n_dp)])
    first = jnp.where(core == 0, mine, other)
    second = jnp.where(core == 0, other, mine)
    return jnp.concatenate([first, second], axis=0), hold


def on_device(inputs, cotangent, control, table_in, table_out, factor_one, second_block_factor, n_dp):
    f32, bf16 = jnp.float32, jnp.bfloat16
    images, rows, width = inputs.shape
    own, blocks, _ = factor_one.shape
    n_seq = blocks // own
    per = own // CHUNKS
    tables = table_in.shape[0]
    one_hot = (control[:, None] == jnp.arange(tables, dtype=jnp.int32)[None, :]).astype(f32)
    gate_in = jnp.dot(one_hot, table_in, precision=lax.Precision.HIGHEST)
    gate_out = jnp.dot(one_hot, table_out, precision=lax.Precision.HIGHEST)
    scaled = (
        inputs.reshape(images, own, blocks, width).astype(f32) * gate_in[:, None, None, :]
    ).astype(bf16)
    f1 = factor_one.reshape(own, n_seq, own, blocks)
    upstream = cotangent.reshape(images, own, blocks, width)

    recv1 = []
    for k in range(CHUNKS):
        mixed = jnp.einsum(
            "asjb,iabd->sajid", f1[:, :, k * per:(k + 1) * per, :], scaled, preferred_element_type=f32
        ).astype(bf16)
        recv1.append(lax.all_to_all(mixed, "seq", 0, 0, tiled=True))

    recv2 = []
    sfg = []
    for k in range(CHUNKS):
        got = recv1[k].reshape(blocks, per, images, width)
        f2 = second_block_factor[k * per:(k + 1) * per]
        mixed_b = jnp.einsum("jpa,ajid->jpid", f2, got, preferred_element_type=f32)
        logistic = jax.nn.sigmoid(mixed_b)
        up = jnp.transpose(upstream[:, k * per:(k + 1) * per], (1, 2, 0, 3))
        value_gradient = (
            up * gate_out[None, None, :, :] * logistic * (1.0 + mixed_b * (1.0 - logistic))
        ).astype(bf16)
        part = jnp.einsum("jpid,ajid->jpa", value_gradient, got, preferred_element_type=f32)
        send = jnp.einsum("jpa,jpid->ajid", f2, value_gradient, preferred_element_type=f32).astype(bf16)
        send = send.reshape(n_seq, own, per, images, width)
        if sfg:
            part, send, sfg[-1] = lax.optimization_barrier((part, send, sfg[-1]))
        else:
            part, send = lax.optimization_barrier((part, send))
        if k < CHUNKS - 1:
            part = dp_sum_halves(part, n_dp)[0]
        sfg.append(part)
        recv2.append(lax.all_to_all(send, "seq", 0, 0, tiled=True))

    grad_one = []
    back_sum = None
    for k in range(CHUNKS):
        got = recv2[k]
        part = jnp.einsum("sajid,iabd->asjb", got, scaled, preferred_element_type=f32)
        if k == 0:
            part, sfg[-1] = lax.optimization_barrier((part, sfg[-1]))
            sfg[-1] = dp_sum_halves(sfg[-1], n_dp)[0]
        if k == CHUNKS - 1:
            reduced, got = dp_sum_halves(part, n_dp, hold=got)
        else:
            reduced, _ = dp_sum_halves(part, n_dp)
        grad_one.append(reduced)
        term = jnp.einsum(
            "asjb,sajid->iabd", f1[:, :, k * per:(k + 1) * per, :], got, preferred_element_type=f32
        )
        back_sum = term if back_sum is None else back_sum + term
    grad_one = jnp.concatenate(grad_one, axis=2).reshape(own, blocks, blocks)
    grad_inputs = (
        (back_sum * gate_in[:, None, None, :]).astype(bf16).reshape(images, rows, width)
    )
    second_factor_gradient = jnp.concatenate(sfg, axis=0)
    return (grad_inputs, grad_one, second_factor_gradient)


def solution(mesh):
    n_dp = mesh.shape["dp"]

    def fn(*args):
        return on_device(*args, n_dp=n_dp)

    return jax.shard_map(
        fn,
        mesh=mesh,
        in_specs=(
            P("dp", "seq", None),
            P("dp", "seq", None),
            P("dp"),
            P(),
            P(),
            P("seq", None, None),
            P("seq", None, None),
        ),
        out_specs=(P("dp", "seq", None), P("seq", None, None), P("seq", None, None)),
        check_vma=False,
    )
```

```python
import jax
import jax.numpy as jnp
from jax import lax
from jax.sharding import PartitionSpec as P

CHUNKS = 2


def dp_sum(x, n_dp):
    step = 1
    while step < n_dp:
        perm = [(i, i ^ step) for i in range(n_dp)]
        x = x + lax.ppermute(x, "dp", perm)
        step *= 2
    return x


def dp_sum_halves(x, n_dp, hold=None):
    if n_dp != 4 or x.shape[0] % 2:
        return dp_sum(x, n_dp), hold
    core = lax.axis_index("dp") % 2
    x = x + lax.ppermute(x, "dp", [(i, i ^ 1) for i in range(n_dp)])
    halves = x.reshape((2, x.shape[0] // 2) + x.shape[1:])
    mine = lax.dynamic_index_in_dim(halves, core, 0, keepdims=False)
    if hold is not None:
        mine, hold = lax.optimization_barrier((mine, hold))
    mine = mine + lax.ppermute(mine, "dp", [(i, i ^ 2) for i in range(n_dp)])
    other = lax.ppermute(mine, "dp", [(i, i ^ 1) for i in range(n_dp)])
    first = jnp.where(core == 0, mine, other)
    second = jnp.where(core == 0, other, mine)
    return jnp.concatenate([first, second], axis=0), hold


def on_device(inputs, cotangent, control, table_in, table_out, factor_one, second_block_factor, n_dp):
    f32, bf16 = jnp.float32, jnp.bfloat16
    images, rows, width = inputs.shape
    own, blocks, _ = factor_one.shape
    n_seq = blocks // own
    per = own // CHUNKS
    tables = table_in.shape[0]
    one_hot = (control[:, None] == jnp.arange(tables, dtype=jnp.int32)[None, :]).astype(f32)
    gate_in = jnp.dot(one_hot, table_in, precision=lax.Precision.HIGHEST)
    gate_out = jnp.dot(one_hot, table_out, precision=lax.Precision.HIGHEST)
    scaled = (
        inputs.reshape(images, own, blocks, width).astype(f32) * gate_in[:, None, None, :]
    ).astype(bf16)
    f1 = factor_one.reshape(own, n_seq, own, blocks)
    upstream = cotangent.reshape(images, own, blocks, width)

    recv1 = []
    for k in range(CHUNKS):
        mixed = jnp.einsum(
            "asjb,iabd->sajid", f1[:, :, k * per:(k + 1) * per, :], scaled, preferred_element_type=f32
        ).astype(bf16)
        recv1.append(lax.all_to_all(mixed, "seq", 0, 0, tiled=True))

    recv2 = []
    sfg = []
    for k in range(CHUNKS):
        got = recv1[k].reshape(blocks, per, images, width)
        f2 = second_block_factor[k * per:(k + 1) * per]
        mixed_b = jnp.einsum("jpa,ajid->jpid", f2, got, preferred_element_type=f32)
        logistic = jax.nn.sigmoid(mixed_b)
        up = jnp.transpose(upstream[:, k * per:(k + 1) * per], (1, 2, 0, 3))
        value_gradient = (
            up * gate_out[None, None, :, :] * logistic * (1.0 + mixed_b * (1.0 - logistic))
        ).astype(bf16)
        part = jnp.einsum("jpid,ajid->jpa", value_gradient, got, preferred_element_type=f32)
        send = jnp.einsum("jpa,jpid->ajid", f2, value_gradient, preferred_element_type=f32).astype(bf16)
        send = send.reshape(n_seq, own, per, images, width)
        if sfg:
            part, send, sfg[-1] = lax.optimization_barrier((part, send, sfg[-1]))
        else:
            part, send = lax.optimization_barrier((part, send))
        if k < CHUNKS - 1:
            part = dp_sum_halves(part, n_dp)[0]
        sfg.append(part)
        recv2.append(lax.all_to_all(send, "seq", 0, 0, tiled=True))

    grad_one = []
    back_sum = None
    for k in range(CHUNKS):
        got = recv2[k]
        if k < CHUNKS - 1:
            part = jnp.einsum("sajid,iabd->asjb", got, scaled, preferred_element_type=f32)
            if k == 0:
                part, sfg[-1] = lax.optimization_barrier((part, sfg[-1]))
                sfg[-1] = dp_sum_halves(sfg[-1], n_dp)[0]
            grad_one.append(dp_sum_halves(part, n_dp)[0])
        else:
            got, grad_one[:], sfg[:] = lax.optimization_barrier((got, list(grad_one), list(sfg)))
            part = jnp.einsum("sajid,iabd->asjb", got, scaled, preferred_element_type=f32)
            reduced, got = dp_sum_halves(part, n_dp, hold=got)
            grad_one.append(reduced)
        term = jnp.einsum(
            "asjb,sajid->iabd", f1[:, :, k * per:(k + 1) * per, :], got, preferred_element_type=f32
        )
        back_sum = term if back_sum is None else back_sum + term
    grad_one = jnp.concatenate(grad_one, axis=2).reshape(own, blocks, blocks)
    grad_inputs = (
        (back_sum * gate_in[:, None, None, :]).astype(bf16).reshape(images, rows, width)
    )
    second_factor_gradient = jnp.concatenate(sfg, axis=0)
    return (grad_inputs, grad_one, second_factor_gradient)


def solution(mesh):
    n_dp = mesh.shape["dp"]

    def fn(*args):
        return on_device(*args, n_dp=n_dp)

    return jax.shard_map(
        fn,
        mesh=mesh,
        in_specs=(
            P("dp", "seq", None),
            P("dp", "seq", None),
            P("dp"),
            P(),
            P(),
            P("seq", None, None),
            P("seq", None, None),
        ),
        out_specs=(P("dp", "seq", None), P("seq", None, None), P("seq", None, None)),
        check_vma=False,
    )
```

```python
import jax
import jax.numpy as jnp
from jax import lax
from jax.sharding import PartitionSpec as P

CHUNKS = 2


def dp_sum(x, n_dp):
    step = 1
    while step < n_dp:
        perm = [(i, i ^ step) for i in range(n_dp)]
        x = x + lax.ppermute(x, "dp", perm)
        step *= 2
    return x


def dp_sum_halves(x, n_dp, hold=None):
    if n_dp != 4 or x.shape[0] % 2:
        return dp_sum(x, n_dp), hold
    core = lax.axis_index("dp") % 2
    halves = x.reshape((2, x.shape[0] // 2) + x.shape[1:])
    mine = lax.dynamic_index_in_dim(halves, core, 0, keepdims=False)
    theirs = lax.dynamic_index_in_dim(halves, 1 - core, 0, keepdims=False)
    mine = mine + lax.ppermute(theirs, "dp", [(i, i ^ 1) for i in range(n_dp)])
    if hold is not None:
        mine, hold = lax.optimization_barrier((mine, hold))
    mine = mine + lax.ppermute(mine, "dp", [(i, i ^ 2) for i in range(n_dp)])
    other = lax.ppermute(mine, "dp", [(i, i ^ 1) for i in range(n_dp)])
    first = jnp.where(core == 0, mine, other)
    second = jnp.where(core == 0, other, mine)
    return jnp.concatenate([first, second], axis=0), hold


def on_device(inputs, cotangent, control, table_in, table_out, factor_one, second_block_factor, n_dp):
    f32, bf16 = jnp.float32, jnp.bfloat16
    images, rows, width = inputs.shape
    own, blocks, _ = factor_one.shape
    n_seq = blocks // own
    per = own // CHUNKS
    tables = table_in.shape[0]
    one_hot = (control[:, None] == jnp.arange(tables, dtype=jnp.int32)[None, :]).astype(f32)
    gate_in = jnp.dot(one_hot, table_in, precision=lax.Precision.HIGHEST)
    gate_out = jnp.dot(one_hot, table_out, precision=lax.Precision.HIGHEST)
    scaled = (
        inputs.reshape(images, own, blocks, width).astype(f32) * gate_in[:, None, None, :]
    ).astype(bf16)
    f1 = factor_one.reshape(own, n_seq, own, blocks)
    upstream = cotangent.reshape(images, own, blocks, width)

    recv1 = []
    for k in range(CHUNKS):
        mixed = jnp.einsum(
            "asjb,iabd->sajid", f1[:, :, k * per:(k + 1) * per, :], scaled, preferred_element_type=f32
        ).astype(bf16)
        recv1.append(lax.all_to_all(mixed, "seq", 0, 0, tiled=True))

    recv2 = []
    sfg = []
    for k in range(CHUNKS):
        got = recv1[k].reshape(blocks, per, images, width)
        f2 = second_block_factor[k * per:(k + 1) * per]
        mixed_b = jnp.einsum("jpa,ajid->jpid", f2, got, preferred_element_type=f32)
        logistic = jax.nn.sigmoid(mixed_b)
        up = jnp.transpose(upstream[:, k * per:(k + 1) * per], (1, 2, 0, 3))
        value_gradient = (
            up * gate_out[None, None, :, :] * logistic * (1.0 + mixed_b * (1.0 - logistic))
        ).astype(bf16)
        part = jnp.einsum("jpid,ajid->jpa", value_gradient, got, preferred_element_type=f32)
        send = jnp.einsum("jpa,jpid->ajid", f2, value_gradient, preferred_element_type=f32).astype(bf16)
        send = send.reshape(n_seq, own, per, images, width)
        if sfg:
            part, send, sfg[-1] = lax.optimization_barrier((part, send, sfg[-1]))
        else:
            part, send = lax.optimization_barrier((part, send))
        if k < CHUNKS - 1:
            part = dp_sum_halves(part, n_dp)[0]
        sfg.append(part)
        recv2.append(lax.all_to_all(send, "seq", 0, 0, tiled=True))

    grad_one = []
    back_sum = None
    for k in range(CHUNKS):
        got = recv2[k]
        if k < CHUNKS - 1:
            part = jnp.einsum("sajid,iabd->asjb", got, scaled, preferred_element_type=f32)
            if k == 0:
                part, sfg[-1] = lax.optimization_barrier((part, sfg[-1]))
                sfg[-1] = dp_sum_halves(sfg[-1], n_dp)[0]
            grad_one.append(dp_sum_halves(part, n_dp)[0])
        else:
            got, grad_one[:], sfg[:] = lax.optimization_barrier((got, list(grad_one), list(sfg)))
            part = jnp.einsum("sajid,iabd->asjb", got, scaled, preferred_element_type=f32)
            reduced, got = dp_sum_halves(part, n_dp, hold=got)
            grad_one.append(reduced)
        term = jnp.einsum(
            "asjb,sajid->iabd", f1[:, :, k * per:(k + 1) * per, :], got, preferred_element_type=f32
        )
        back_sum = term if back_sum is None else back_sum + term
    grad_one = jnp.concatenate(grad_one, axis=2).reshape(own, blocks, blocks)
    grad_inputs = (
        (back_sum * gate_in[:, None, None, :]).astype(bf16).reshape(images, rows, width)
    )
    second_factor_gradient = jnp.concatenate(sfg, axis=0)
    return (grad_inputs, grad_one, second_factor_gradient)


def solution(mesh):
    n_dp = mesh.shape["dp"]

    def fn(*args):
        return on_device(*args, n_dp=n_dp)

    return jax.shard_map(
        fn,
        mesh=mesh,
        in_specs=(
            P("dp", "seq", None),
            P("dp", "seq", None),
            P("dp"),
            P(),
            P(),
            P("seq", None, None),
            P("seq", None, None),
        ),
        out_specs=(P("dp", "seq", None), P("seq", None, None), P("seq", None, None)),
        check_vma=False,
    )
```

```python
import jax
import jax.numpy as jnp
from jax import lax
from jax.sharding import PartitionSpec as P

CHUNKS = 2


def dp_sum(x, n_dp):
    step = 1
    while step < n_dp:
        perm = [(i, i ^ step) for i in range(n_dp)]
        x = x + lax.ppermute(x, "dp", perm)
        step *= 2
    return x


def dp_sum_halves(x, n_dp, hold=None):
    if n_dp != 4 or x.shape[0] % 2:
        return dp_sum(x, n_dp), hold
    core = lax.axis_index("dp") % 2
    x = x + lax.ppermute(x, "dp", [(i, i ^ 1) for i in range(n_dp)])
    halves = x.reshape((2, x.shape[0] // 2) + x.shape[1:])
    mine = lax.dynamic_index_in_dim(halves, core, 0, keepdims=False)
    if hold is not None:
        mine, hold = lax.optimization_barrier((mine, hold))
    mine = mine + lax.ppermute(mine, "dp", [(i, i ^ 2) for i in range(n_dp)])
    other = lax.ppermute(mine, "dp", [(i, i ^ 1) for i in range(n_dp)])
    first = jnp.where(core == 0, mine, other)
    second = jnp.where(core == 0, other, mine)
    return jnp.concatenate([first, second], axis=0), hold


def on_device(inputs, cotangent, control, table_in, table_out, factor_one, second_block_factor, n_dp):
    f32, bf16 = jnp.float32, jnp.bfloat16
    images, rows, width = inputs.shape
    own, blocks, _ = factor_one.shape
    n_seq = blocks // own
    per = own // CHUNKS
    tables = table_in.shape[0]
    one_hot = (control[:, None] == jnp.arange(tables, dtype=jnp.int32)[None, :]).astype(f32)
    gate_in = jnp.dot(one_hot, table_in, precision=lax.Precision.HIGHEST)
    gate_out = jnp.dot(one_hot, table_out, precision=lax.Precision.HIGHEST)
    scaled = (
        inputs.reshape(images, own, blocks, width).astype(f32) * gate_in[:, None, None, :]
    ).astype(bf16)
    f1 = factor_one.reshape(own, n_seq, own, blocks)
    upstream = cotangent.reshape(images, own, blocks, width)

    recv1 = []
    for k in range(CHUNKS):
        mixed = jnp.einsum(
            "asjb,iabd->sajid", f1[:, :, k * per:(k + 1) * per, :], scaled, preferred_element_type=f32
        ).astype(bf16)
        flat = mixed.reshape(n_seq, own * per * images, width)
        recv1.append(
            lax.all_to_all(flat, "seq", 0, 0, tiled=True).reshape(n_seq, own, per, images, width)
        )

    recv2 = []
    sfg = []
    for k in range(CHUNKS):
        got = recv1[k].reshape(blocks, per, images, width)
        f2 = second_block_factor[k * per:(k + 1) * per]
        mixed_b = jnp.einsum("jpa,ajid->jpid", f2, got, preferred_element_type=f32)
        logistic = jax.nn.sigmoid(mixed_b)
        up = jnp.transpose(upstream[:, k * per:(k + 1) * per], (1, 2, 0, 3))
        value_gradient = (
            up * gate_out[None, None, :, :] * logistic * (1.0 + mixed_b * (1.0 - logistic))
        ).astype(bf16)
        part = jnp.einsum("jpid,ajid->jpa", value_gradient, got, preferred_element_type=f32)
        send = jnp.einsum("jpa,jpid->ajid", f2, value_gradient, preferred_element_type=f32).astype(bf16)
        send = send.reshape(n_seq, own, per, images, width)
        if sfg:
            part, send, sfg[-1] = lax.optimization_barrier((part, send, sfg[-1]))
        else:
            part, send = lax.optimization_barrier((part, send))
        if k < CHUNKS - 1:
            part = dp_sum_halves(part, n_dp)[0]
        sfg.append(part)
        recv2.append(lax.all_to_all(send, "seq", 0, 0, tiled=True))

    grad_one = []
    back_sum = None
    for k in range(CHUNKS):
        got = recv2[k]
        if k < CHUNKS - 1:
            part = jnp.einsum("sajid,iabd->asjb", got, scaled, preferred_element_type=f32)
            if k == 0:
                part, sfg[-1] = lax.optimization_barrier((part, sfg[-1]))
                sfg[-1] = dp_sum_halves(sfg[-1], n_dp)[0]
            grad_one.append(dp_sum_halves(part, n_dp)[0])
        else:
            got, grad_one[:], sfg[:] = lax.optimization_barrier((got, list(grad_one), list(sfg)))
            part = jnp.einsum("sajid,iabd->asjb", got, scaled, preferred_element_type=f32)
            reduced, got = dp_sum_halves(part, n_dp, hold=got)
            grad_one.append(reduced)
        term = jnp.einsum(
            "asjb,sajid->iabd", f1[:, :, k * per:(k + 1) * per, :], got, preferred_element_type=f32
        )
        back_sum = term if back_sum is None else back_sum + term
    grad_one = jnp.concatenate(grad_one, axis=2).reshape(own, blocks, blocks)
    grad_inputs = (
        (back_sum * gate_in[:, None, None, :]).astype(bf16).reshape(images, rows, width)
    )
    second_factor_gradient = jnp.concatenate(sfg, axis=0)
    return (grad_inputs, grad_one, second_factor_gradient)


def solution(mesh):
    n_dp = mesh.shape["dp"]

    def fn(*args):
        return on_device(*args, n_dp=n_dp)

    return jax.shard_map(
        fn,
        mesh=mesh,
        in_specs=(
            P("dp", "seq", None),
            P("dp", "seq", None),
            P("dp"),
            P(),
            P(),
            P("seq", None, None),
            P("seq", None, None),
        ),
        out_specs=(P("dp", "seq", None), P("seq", None, None), P("seq", None, None)),
        check_vma=False,
    )
```

```python
import jax
import jax.numpy as jnp
from jax import lax
from jax.sharding import PartitionSpec as P

CHUNKS = 2


def dp_sum(x, n_dp):
    step = 1
    while step < n_dp:
        perm = [(i, i ^ step) for i in range(n_dp)]
        x = x + lax.ppermute(x, "dp", perm)
        step *= 2
    return x


def dp_sum_halves(x, n_dp, hold=None):
    if n_dp != 4 or x.shape[0] % 2:
        return dp_sum(x, n_dp), hold
    core = lax.axis_index("dp") % 2
    x = x + lax.ppermute(x, "dp", [(i, i ^ 1) for i in range(n_dp)])
    halves = x.reshape((2, x.shape[0] // 2) + x.shape[1:])
    mine = lax.dynamic_index_in_dim(halves, core, 0, keepdims=False)
    if hold is not None:
        mine, hold = lax.optimization_barrier((mine, hold))
    mine = mine + lax.ppermute(mine, "dp", [(i, i ^ 2) for i in range(n_dp)])
    other = lax.ppermute(mine, "dp", [(i, i ^ 1) for i in range(n_dp)])
    first = jnp.where(core == 0, mine, other)
    second = jnp.where(core == 0, other, mine)
    return jnp.concatenate([first, second], axis=0), hold


def on_device(inputs, cotangent, control, table_in, table_out, factor_one, second_block_factor, n_dp):
    f32, bf16 = jnp.float32, jnp.bfloat16
    images, rows, width = inputs.shape
    own, blocks, _ = factor_one.shape
    n_seq = blocks // own
    per = own // CHUNKS
    tables = table_in.shape[0]
    one_hot = (control[:, None] == jnp.arange(tables, dtype=jnp.int32)[None, :]).astype(f32)
    gate_in = jnp.dot(one_hot, table_in, precision=lax.Precision.HIGHEST)
    gate_out = jnp.dot(one_hot, table_out, precision=lax.Precision.HIGHEST)
    scaled = (
        inputs.reshape(images, own, blocks, width).astype(f32) * gate_in[:, None, None, :]
    ).astype(bf16)
    f1 = factor_one.reshape(own, n_seq, own, blocks)
    upstream = cotangent.reshape(images, own, blocks, width)

    recv1 = []
    for k in range(CHUNKS):
        mixed = jnp.einsum(
            "asjb,iabd->sajid", f1[:, :, k * per:(k + 1) * per, :], scaled, preferred_element_type=f32
        ).astype(bf16)
        flat = mixed.reshape(n_seq, own * per * images, width)
        recv1.append(
            lax.all_to_all(flat, "seq", 0, 0, tiled=True).reshape(n_seq, own, per, images, width)
        )

    recv2 = []
    sfg = []
    for k in range(CHUNKS):
        got = recv1[k].reshape(blocks, per, images, width)
        f2 = second_block_factor[k * per:(k + 1) * per]
        mixed_b = jnp.einsum("jpa,ajid->jpid", f2, got, preferred_element_type=f32)
        logistic = jax.nn.sigmoid(mixed_b)
        up = jnp.transpose(upstream[:, k * per:(k + 1) * per], (1, 2, 0, 3))
        value_gradient = (
            up * gate_out[None, None, :, :] * logistic * (1.0 + mixed_b * (1.0 - logistic))
        ).astype(bf16)
        part = jnp.einsum("jpid,ajid->jpa", value_gradient, got, preferred_element_type=f32)
        send = jnp.einsum("jpa,jpid->ajid", f2, value_gradient, preferred_element_type=f32).astype(bf16)
        send = send.reshape(n_seq, own, per, images, width)
        if sfg:
            part, send, sfg[-1] = lax.optimization_barrier((part, send, sfg[-1]))
        else:
            part, send = lax.optimization_barrier((part, send))
        if k < CHUNKS - 1:
            part = dp_sum_halves(part, n_dp)[0]
        sfg.append(part)
        recv2.append(lax.all_to_all(send, "seq", 0, 0, tiled=True))

    grad_one = []
    back_sum = None
    for k in range(CHUNKS):
        got = recv2[k]
        if k < CHUNKS - 1:
            part = jnp.einsum("sajid,iabd->asjb", got, scaled, preferred_element_type=f32)
            if k == 0:
                part, sfg[-1] = lax.optimization_barrier((part, sfg[-1]))
                sfg[-1] = dp_sum_halves(sfg[-1], n_dp)[0]
            grad_one.append(dp_sum_halves(part, n_dp)[0])
        else:
            got, grad_one[:], sfg[:] = lax.optimization_barrier((got, list(grad_one), list(sfg)))
            part = jnp.einsum("sajid,iabd->asjb", got, scaled, preferred_element_type=f32)
            if n_dp == 4 and own % 2 == 0:
                core = lax.axis_index("dp") % 2
                x = part + lax.ppermute(part, "dp", [(i, i ^ 1) for i in range(n_dp)])
                halves = x.reshape((2, x.shape[0] // 2) + x.shape[1:])
                mine = lax.dynamic_index_in_dim(halves, core, 0, keepdims=False)
                mine, got = lax.optimization_barrier((mine, got))
                mine = mine + lax.ppermute(mine, "dp", [(i, i ^ 2) for i in range(n_dp)])
                term = jnp.einsum(
                    "asjb,sajid->iabd", f1[:, :, k * per:, :], got, preferred_element_type=f32
                )
                back_sum = back_sum + term
                grad_inputs = (
                    (back_sum * gate_in[:, None, None, :]).astype(bf16).reshape(images, rows, width)
                )
                mine, grad_inputs = lax.optimization_barrier((mine, grad_inputs))
                other = lax.ppermute(mine, "dp", [(i, i ^ 1) for i in range(n_dp)])
                first = jnp.where(core == 0, mine, other)
                second = jnp.where(core == 0, other, mine)
                grad_one.append(jnp.concatenate([first, second], axis=0))
                break
            reduced, got = dp_sum_halves(part, n_dp, hold=got)
            grad_one.append(reduced)
        term = jnp.einsum(
            "asjb,sajid->iabd", f1[:, :, k * per:(k + 1) * per, :], got, preferred_element_type=f32
        )
        back_sum = term if back_sum is None else back_sum + term
    else:
        grad_inputs = (
            (back_sum * gate_in[:, None, None, :]).astype(bf16).reshape(images, rows, width)
        )
    grad_one = jnp.concatenate(grad_one, axis=2).reshape(own, blocks, blocks)
    second_factor_gradient = jnp.concatenate(sfg, axis=0)
    return (grad_inputs, grad_one, second_factor_gradient)


def solution(mesh):
    n_dp = mesh.shape["dp"]

    def fn(*args):
        return on_device(*args, n_dp=n_dp)

    return jax.shard_map(
        fn,
        mesh=mesh,
        in_specs=(
            P("dp", "seq", None),
            P("dp", "seq", None),
            P("dp"),
            P(),
            P(),
            P("seq", None, None),
            P("seq", None, None),
        ),
        out_specs=(P("dp", "seq", None), P("seq", None, None), P("seq", None, None)),
        check_vma=False,
    )
```

```python
import jax
import jax.numpy as jnp
from jax import lax
from jax.experimental.layout import Layout, with_layout_constraint
from jax.sharding import PartitionSpec as P

CHUNKS = 2


def dp_sum(x, n_dp):
    step = 1
    while step < n_dp:
        perm = [(i, i ^ step) for i in range(n_dp)]
        x = x + lax.ppermute(x, "dp", perm)
        step *= 2
    return x


def dp_sum_halves(x, n_dp, hold=None):
    if n_dp != 4 or x.shape[0] % 2:
        return dp_sum(x, n_dp), hold
    core = lax.axis_index("dp") % 2
    x = x + lax.ppermute(x, "dp", [(i, i ^ 1) for i in range(n_dp)])
    halves = x.reshape((2, x.shape[0] // 2) + x.shape[1:])
    mine = lax.dynamic_index_in_dim(halves, core, 0, keepdims=False)
    if hold is not None:
        mine, hold = lax.optimization_barrier((mine, hold))
    mine = mine + lax.ppermute(mine, "dp", [(i, i ^ 2) for i in range(n_dp)])
    other = lax.ppermute(mine, "dp", [(i, i ^ 1) for i in range(n_dp)])
    first = jnp.where(core == 0, mine, other)
    second = jnp.where(core == 0, other, mine)
    return jnp.concatenate([first, second], axis=0), hold


def on_device(inputs, cotangent, control, table_in, table_out, factor_one, second_block_factor, n_dp):
    f32, bf16 = jnp.float32, jnp.bfloat16
    images, rows, width = inputs.shape
    own, blocks, _ = factor_one.shape
    n_seq = blocks // own
    per = own // CHUNKS
    tables = table_in.shape[0]
    one_hot = (control[:, None] == jnp.arange(tables, dtype=jnp.int32)[None, :]).astype(f32)
    gate_in = jnp.dot(one_hot, table_in, precision=lax.Precision.HIGHEST)
    gate_out = jnp.dot(one_hot, table_out, precision=lax.Precision.HIGHEST)
    scaled = (
        inputs.reshape(images, own, blocks, width).astype(f32) * gate_in[:, None, None, :]
    ).astype(bf16)
    f1 = factor_one.reshape(own, n_seq, own, blocks)
    upstream = cotangent.reshape(images, own, blocks, width)

    recv1 = []
    for k in range(CHUNKS):
        mixed = jnp.einsum(
            "asjb,iabd->sajid", f1[:, :, k * per:(k + 1) * per, :], scaled, preferred_element_type=f32
        ).astype(bf16)
        flat = mixed.reshape(n_seq, own * per * images, width)
        recv1.append(
            lax.all_to_all(flat, "seq", 0, 0, tiled=True).reshape(n_seq, own, per, images, width)
        )

    recv2 = []
    sfg = []
    for k in range(CHUNKS):
        got = recv1[k].reshape(blocks, per, images, width)
        f2 = second_block_factor[k * per:(k + 1) * per]
        mixed_b = jnp.einsum("jpa,ajid->jpid", f2, got, preferred_element_type=f32)
        logistic = jax.nn.sigmoid(mixed_b)
        up = jnp.transpose(upstream[:, k * per:(k + 1) * per], (1, 2, 0, 3))
        value_gradient = (
            up * gate_out[None, None, :, :] * logistic * (1.0 + mixed_b * (1.0 - logistic))
        ).astype(bf16)
        part = jnp.einsum("jpid,ajid->jpa", value_gradient, got, preferred_element_type=f32)
        send = jnp.einsum("jpa,jpid->ajid", f2, value_gradient, preferred_element_type=f32).astype(bf16)
        send = send.reshape(n_seq, own, per, images, width)
        if sfg:
            part, send, sfg[-1] = lax.optimization_barrier((part, send, sfg[-1]))
        else:
            part, send = lax.optimization_barrier((part, send))
        if k < CHUNKS - 1:
            part = dp_sum_halves(part, n_dp)[0]
        sfg.append(part)
        recv2.append(lax.all_to_all(send, "seq", 0, 0, tiled=True))

    grad_one = []
    back_sum = None
    for k in range(CHUNKS):
        got = recv2[k]
        if k < CHUNKS - 1:
            part = jnp.einsum("sajid,iabd->asjb", got, scaled, preferred_element_type=f32)
            if k == 0:
                part, sfg[-1] = lax.optimization_barrier((part, sfg[-1]))
                sfg[-1] = dp_sum_halves(sfg[-1], n_dp)[0]
            grad_one.append(dp_sum_halves(part, n_dp)[0])
        else:
            got, grad_one[:], sfg[:] = lax.optimization_barrier((got, list(grad_one), list(sfg)))
            part = jnp.einsum("sajid,iabd->asjb", got, scaled, preferred_element_type=f32)
            if n_dp == 4 and own % 2 == 0:
                core = lax.axis_index("dp") % 2
                x = part + lax.ppermute(part, "dp", [(i, i ^ 1) for i in range(n_dp)])
                halves = x.reshape((2, x.shape[0] // 2) + x.shape[1:])
                mine = lax.dynamic_index_in_dim(halves, core, 0, keepdims=False)
                mine, got = lax.optimization_barrier((mine, got))
                mine = mine + lax.ppermute(mine, "dp", [(i, i ^ 2) for i in range(n_dp)])
                term = jnp.einsum(
                    "asjb,sajid->iabd", f1[:, :, k * per:, :], got, preferred_element_type=f32
                )
                back_sum = back_sum + term
                grad_inputs = (
                    (back_sum * gate_in[:, None, None, :]).astype(bf16).reshape(images, rows, width)
                )
                mine, grad_inputs = lax.optimization_barrier((mine, grad_inputs))
                other = lax.ppermute(mine, "dp", [(i, i ^ 1) for i in range(n_dp)])
                first = jnp.where(core == 0, mine, other)
                second = jnp.where(core == 0, other, mine)
                grad_one.append(jnp.concatenate([first, second], axis=0))
                break
            reduced, got = dp_sum_halves(part, n_dp, hold=got)
            grad_one.append(reduced)
        term = jnp.einsum(
            "asjb,sajid->iabd", f1[:, :, k * per:(k + 1) * per, :], got, preferred_element_type=f32
        )
        back_sum = term if back_sum is None else back_sum + term
    else:
        grad_inputs = (
            (back_sum * gate_in[:, None, None, :]).astype(bf16).reshape(images, rows, width)
        )
    grad_one = jnp.concatenate(grad_one, axis=2)
    grad_one = with_layout_constraint(grad_one, Layout(major_to_minor=(0, 1, 2, 3)))
    grad_one = grad_one.reshape(own, blocks, blocks)
    second_factor_gradient = jnp.concatenate(sfg, axis=0)
    return (grad_inputs, grad_one, second_factor_gradient)


def solution(mesh):
    n_dp = mesh.shape["dp"]

    def fn(*args):
        return on_device(*args, n_dp=n_dp)

    return jax.shard_map(
        fn,
        mesh=mesh,
        in_specs=(
            P("dp", "seq", None),
            P("dp", "seq", None),
            P("dp"),
            P(),
            P(),
            P("seq", None, None),
            P("seq", None, None),
        ),
        out_specs=(P("dp", "seq", None), P("seq", None, None), P("seq", None, None)),
        check_vma=False,
    )
```
